512 devices in a mesh: row: 32 (over z, core), band: 16 (over y, x).
Axes of the slice: x: 4, y: 4, z: 16, core: 2. Of those that a mesh axis runs over, the one named last changes fastest.
Arguments:
- band_blocks: bfloat16 [1024, 16, 128, 128], P('row', 'band'), may hold values from 0 to 0.006591797, as said below
- distant_block_slots: bfloat16 [32, 16, 32, 2, 128, 128], P('row', 'band'), may hold values from 0 to 0.00033203125, as said below
- far_rows: int32 [32, 16, 32, 2], P('row', 'band'), may hold values from 0 to 31
- far_columns: int32 [32, 16, 32, 2], P('row', 'band'), may hold values from 0 to 31
- far_counts: int32 [32, 16, 32], P('row', 'band'), may hold values from 0 to 2, as said below
Outputs:
- scaling: float32 [1024, 128], P('row')
- residual: float32 [1024, 128], P('row')
The draws below stay inside these ranges and needn't reach their ends.
Inputs may be any that keep to these rules, and one draw needn't show every extreme that they name: `band_blocks`: positive entries; offset-0 blocks symmetric. `distant_block_slots`: positive entries. `far_counts`: some target range receives 2 live slots from every device.
All inputs are finite; a program needn't handle non-finite values.
Results may differ from the reference program's by a relative error of at most 0.0116.
The reference program's roundings to bfloat16 on the way count: a program that leaves them out, or rounds other values in their place, can miss the bound.
Values may be sent and summed in bfloat16 or wider, within the bound.
No kernel may reach another device: no remote copies, remote signals or barrier semaphores. Data moves between devices by JAX's collectives and lax.ppermute only.
A program may use at most 64 MiB of HBM per device.

```python
import math
import jax
import jax.numpy as jnp
from jax import lax

BLK = 128
BR_DEV = 32
CAP = 2
OUTER = 2
INNER = 2
N_ROW = 32
N_BAND = 16


def bin_bias(key):
    subkey = jax.random.fold_in(key, 11)
    length = N_ROW * BR_DEV * BLK
    values = jnp.exp(jax.random.uniform(subkey, (length,), jnp.float32, math.log(0.3), math.log(3.0)))
    return values.reshape(N_ROW * BR_DEV, BLK)


def far_layout(key):
    subkey = jax.random.fold_in(key, 21)
    first, second, third, fourth = jax.random.split(subkey, 4)
    shape = (N_ROW, N_BAND, N_ROW, CAP)
    local_row_values = jax.random.randint(first, shape, 0, BR_DEV).astype(jnp.int32)
    columns_local = jax.random.randint(second, shape, 0, BR_DEV).astype(jnp.int32)
    counts = jax.random.randint(third, (N_ROW, N_BAND, N_ROW), 0, CAP + 1).astype(jnp.int32)
    selected_slot = jax.random.randint(fourth, (), 0, N_ROW).astype(jnp.int32)
    targets = jnp.arange(N_ROW).astype(jnp.int32)[None, None, :]
    counts = jnp.where(targets == selected_slot, CAP, counts).astype(jnp.int32)
    return (local_row_values, columns_local, counts)


def draw_band_blocks(key, part):
    block_count = N_ROW * BR_DEV
    bias = bin_bias(key)
    noise = jax.random.uniform(jax.random.fold_in(key, 12), (block_count, N_BAND, BLK, BLK), jnp.float32, 0.5, 1.5)
    diagonal = 0.5 * (noise[:, 0] + jnp.swapaxes(noise[:, 0], 1, 2))
    noise = noise.at[:, 0].set(diagonal)
    col_index = (jnp.arange(block_count)[:, None] + jnp.arange(N_BAND)[None, :]) % block_count
    row_bias = bias[:, None, :, None]
    col_bias = bias[col_index][:, :, None, :]
    distance = jnp.abs(jnp.arange(N_BAND)[:, None, None] * BLK + jnp.arange(BLK)[None, None, :] - jnp.arange(BLK)[None, :, None]).astype(jnp.float32)
    decay = 1.0 / (1.0 + distance / BLK)
    values = noise * row_bias * col_bias * decay[None] / (BLK * N_BAND)
    return values.astype(jnp.bfloat16)


def draw_distant_block_slots(key, part):
    local_row_values, columns_local, counts = far_layout(key)
    bias = bin_bias(key)
    global_rows = jnp.arange(N_ROW)[:, None, None, None] * BR_DEV + local_row_values
    global_cols = jnp.arange(N_ROW)[None, None, :, None] * BR_DEV + columns_local
    noise = jax.random.uniform(jax.random.fold_in(key, 22), (N_ROW, N_BAND, N_ROW, CAP, BLK, BLK), jnp.float32, 0.5, 1.5)
    values = noise * bias[global_rows][..., :, None] * bias[global_cols][..., None, :] * (0.05 / (BLK * N_BAND))
    return values.astype(jnp.bfloat16)


def draw_far_rows(key, part):
    return far_layout(key)[0]


def draw_far_columns(key, part):
    return far_layout(key)[1]


def draw_far_counts(key, part):
    return far_layout(key)[2]


def setup_inputs(seed: int = 0) -> dict:
    streams_of = jax.random.split(jax.random.key(seed), 6)
    band_blocks = draw_band_blocks(jax.random.fold_in(streams_of[5], 71), 0)
    distant_block_slots = draw_distant_block_slots(jax.random.fold_in(streams_of[5], 71), 0)
    far_rows = draw_far_rows(jax.random.fold_in(streams_of[5], 71), 0)
    far_columns = draw_far_columns(jax.random.fold_in(streams_of[5], 71), 0)
    far_counts = draw_far_counts(jax.random.fold_in(streams_of[5], 71), 0)
    return dict(band_blocks=band_blocks, distant_block_slots=distant_block_slots, far_rows=far_rows, far_columns=far_columns, far_counts=far_counts)


def multiply(vector, band_blocks, distant_block_slots, far_rows, far_columns, far_counts):
    block_count = vector.shape[0]
    narrow_band_part = lax.optimization_barrier(vector.astype(jnp.bfloat16)).astype(jnp.float32)
    accumulated = jnp.zeros((block_count + N_BAND, BLK), jnp.float32)
    padded = jnp.concatenate([narrow_band_part, jnp.zeros((N_BAND, BLK), jnp.float32)], 0)
    block_ids = jnp.arange(block_count).astype(jnp.int32)
    for offset in range(N_BAND):
        blocks = band_blocks[:, offset].astype(jnp.float32)
        valid_mask = (block_ids + offset < block_count).astype(jnp.float32)[:, None]
        columns = padded[offset:offset + block_count]
        forward = jnp.einsum('kij,kj->ki', blocks, columns, precision=lax.Precision.HIGHEST) * valid_mask
        accumulated = accumulated.at[:block_count].add(forward)
        if offset > 0:
            backward = jnp.einsum('kij,ki->kj', blocks, narrow_band_part, precision=lax.Precision.HIGHEST) * valid_mask
            accumulated = accumulated.at[offset:offset + block_count].add(backward)

    def per_source(items):
        blocks, local_row_values, columns_local, counts, source = items
        live_mask = (jnp.arange(CAP).astype(jnp.int32)[None, None, :] < counts[:, :, None]).astype(jnp.float32)[..., None]
        global_rows = source * BR_DEV + local_row_values
        global_cols = jnp.arange(N_ROW).astype(jnp.int32)[None, :, None] * BR_DEV + columns_local
        wide_blocks = blocks.astype(jnp.float32)
        forward = jnp.einsum('bdcij,bdcj->bdci', wide_blocks, narrow_band_part[global_cols], precision=lax.Precision.HIGHEST) * live_mask
        backward = jnp.einsum('bdcij,bdci->bdcj', wide_blocks, narrow_band_part[global_rows], precision=lax.Precision.HIGHEST) * live_mask
        first = jax.ops.segment_sum(forward.reshape(-1, BLK), global_rows.reshape(-1), block_count)
        second = jax.ops.segment_sum(backward.reshape(-1, BLK), global_cols.reshape(-1), block_count)
        return first + second
    partials = lax.map(per_source, (distant_block_slots, far_rows, far_columns, far_counts, jnp.arange(N_ROW).astype(jnp.int32)))
    return accumulated[:block_count] + lax.optimization_barrier(jnp.sum(partials, axis=0))

def reference(band_blocks, distant_block_slots, far_rows, far_columns, far_counts):
    block_count = band_blocks.shape[0]

    def product(vector):
        return multiply(vector, band_blocks, distant_block_slots, far_rows, far_columns, far_counts)
    row_sums = product(jnp.ones((block_count, BLK), jnp.float32))
    scaling = 1.0 / jnp.sqrt(row_sums)
    residual = jnp.zeros_like(scaling)
    for outer_step in range(OUTER):
        balance = scaling * product(scaling)
        residual = 1.0 - balance
        scaled = residual / balance
        direction = scaled
        current_residual_product = jnp.sum(residual * scaled)
        growth = jnp.ones_like(scaling)
        for inner_step in range(INNER):
            curved = scaling * product(scaling * direction) + balance * direction
            step_size = current_residual_product / jnp.sum(direction * curved)
            growth = growth + step_size * direction
            residual = residual - step_size * curved
            if inner_step + 1 < INNER:
                scaled = residual / balance
                rho_next = jnp.sum(residual * scaled)
                direction = scaled + rho_next / current_residual_product * direction
                current_residual_product = rho_next
        scaling = scaling * growth
    return (scaling, residual)
```

```python
import jax
import jax.numpy as jnp
from jax import lax
from jax.sharding import PartitionSpec as P

OUTER = 2
INNER = 2


def shifted(value, axis, steps):
    count = lax.axis_size(axis)
    leading, last = (max(0, -steps), min(count, count - steps))
    return lax.ppermute(value, axis, [(source, source + steps) for source in range(leading, last)])


def all_sum(value, axis):
    count = lax.axis_size(axis)
    if count & (count - 1):
        return lax.psum(value, axis)
    step = 1
    while step < count:
        value = value + lax.ppermute(value, axis, [(source, source ^ step) for source in range(count)])
        step *= 2
    return value


def on_device(band_blocks, distant_block_slots, far_rows, far_columns, far_counts):
    rows_dev = band_blocks.shape[0]
    block_size = band_blocks.shape[2]
    band_count = lax.axis_size("band")
    row_count = lax.axis_size("row")
    offset = lax.axis_index("band")
    row_index = lax.axis_index("row")
    blocks = band_blocks[:, 0]
    distant_local_part = distant_block_slots[0, 0]
    local_row_values = far_rows[0, 0]
    columns_local = far_columns[0, 0]
    counts = far_counts[0, 0]
    slots = local_row_values.shape[1]
    live_mask = (jnp.arange(slots)[None, :] < counts[:, None]).astype(jnp.float32)[..., None]
    block_ids = row_index * rows_dev + jnp.arange(rows_dev)
    valid_mask = (block_ids + offset < row_count * rows_dev).astype(jnp.float32)[:, None]
    upper_mask = (offset > 0).astype(jnp.float32)
    wanted = lax.all_to_all(columns_local, "row", split_axis=0, concat_axis=0, tiled=True)
    targets = jnp.arange(rows_dev)[None, :]
    selection_output = (wanted.reshape(-1)[:, None] == targets).astype(jnp.float32)
    pick_in = (local_row_values.reshape(-1)[:, None] == targets).astype(jnp.float32)

    def multiply(vector):
        narrow_band_part = vector.astype(jnp.bfloat16)
        ahead_rows = shifted(narrow_band_part[:band_count], "row", -1)
        extended = jnp.concatenate([narrow_band_part, ahead_rows], 0)
        columns = lax.dynamic_slice_in_dim(extended, offset, rows_dev, 0)
        forward = (
            jnp.einsum("kij,kj->ki", blocks, columns, preferred_element_type=jnp.float32)
            * valid_mask
        )
        backward = jnp.einsum(
            "kij,ki->kj", blocks, narrow_band_part, preferred_element_type=jnp.float32
        ) * (valid_mask * upper_mask)
        spread = lax.dynamic_update_slice_in_dim(
            jnp.zeros((rows_dev + band_count, block_size), jnp.float32), backward, offset, 0
        )
        outgoing = narrow_band_part[wanted]
        gathered_values = lax.all_to_all(outgoing, "row", split_axis=0, concat_axis=0, tiled=True)
        far_forward = (
            jnp.einsum(
                "oqht,oqt->oqh",
                distant_local_part,
                gathered_values,
                preferred_element_type=jnp.float32,
            )
            * live_mask
        )
        far_backward = (
            jnp.einsum(
                "nquo,nqu->nqo",
                distant_local_part,
                narrow_band_part[local_row_values],
                preferred_element_type=jnp.float32,
            )
            * live_mask
        )
        returned = lax.all_to_all(far_backward, "row", split_axis=0, concat_axis=0, tiled=True)
        summed = forward + spread[:rows_dev]
        summed = summed + jnp.dot(
            pick_in.T, far_forward.reshape(-1, block_size), precision=lax.Precision.HIGHEST
        )
        summed = summed + jnp.dot(
            selection_output.T, returned.reshape(-1, block_size), precision=lax.Precision.HIGHEST
        )
        carried = shifted(spread[rows_dev:], "row", 1)
        summed = jnp.concatenate([summed[:band_count] + carried, summed[band_count:]], 0)
        return all_sum(summed, "band")

    row_sums = multiply(jnp.ones((rows_dev, block_size), jnp.float32))
    scaling = 1.0 / jnp.sqrt(row_sums)
    residual = jnp.zeros_like(scaling)
    for outer_step in range(OUTER):
        balance = scaling * multiply(scaling)
        residual = 1.0 - balance
        scaled = residual / balance
        direction = scaled
        current_residual_product = all_sum(jnp.sum(residual * scaled), "row")
        growth = jnp.ones_like(scaling)
        for inner_step in range(INNER):
            curved = scaling * multiply(scaling * direction) + balance * direction
            curvature = all_sum(jnp.sum(direction * curved), "row")
            step_size = current_residual_product / curvature
            growth = growth + step_size * direction
            residual = residual - step_size * curved
            if inner_step + 1 < INNER:
                scaled = residual / balance
                rho_next = all_sum(jnp.sum(residual * scaled), "row")
                direction = scaled + rho_next / current_residual_product * direction
                current_residual_product = rho_next
        scaling = scaling * growth
    return (scaling, residual)


def solution(mesh):
    return jax.shard_map(
        on_device,
        mesh=mesh,
        in_specs=(
            P("row", "band", None, None),
            P("row", "band", None, None, None, None),
            P("row", "band", None, None),
            P("row", "band", None, None),
            P("row", "band", None),
        ),
        out_specs=(P("row", None), P("row", None)),
        check_vma=False,
    )
```

```python
import jax
import jax.numpy as jnp
from jax import lax
from jax.sharding import PartitionSpec as P

OUTER = 2
INNER = 2


def shifted(value, axis, steps):
    count = lax.axis_size(axis)
    leading, last = (max(0, -steps), min(count, count - steps))
    return lax.ppermute(value, axis, [(source, source + steps) for source in range(leading, last)])


def all_sum(value, axis):
    count = lax.axis_size(axis)
    copies = jnp.broadcast_to(value[None], (count,) + value.shape)
    return jnp.sum(lax.all_to_all(copies, axis, 0, 0, tiled=True), 0)


def on_device(band_blocks, distant_block_slots, far_rows, far_columns, far_counts):
    rows_dev = band_blocks.shape[0]
    block_size = band_blocks.shape[2]
    band_count = lax.axis_size("band")
    row_count = lax.axis_size("row")
    offset = lax.axis_index("band")
    row_index = lax.axis_index("row")
    blocks = band_blocks[:, 0]
    distant_local_part = distant_block_slots[0, 0]
    local_row_values = far_rows[0, 0]
    columns_local = far_columns[0, 0]
    counts = far_counts[0, 0]
    slots = local_row_values.shape[1]
    live_mask = (jnp.arange(slots)[None, :] < counts[:, None]).astype(jnp.float32)[..., None]
    block_ids = row_index * rows_dev + jnp.arange(rows_dev)
    valid_mask = (block_ids + offset < row_count * rows_dev).astype(jnp.float32)[:, None]
    upper_mask = (offset > 0).astype(jnp.float32)
    wanted = lax.all_to_all(columns_local, "row", split_axis=0, concat_axis=0, tiled=True)
    targets = jnp.arange(rows_dev)[None, :]
    selection_output = (wanted.reshape(-1)[:, None] == targets).astype(jnp.float32)
    pick_in = (local_row_values.reshape(-1)[:, None] == targets).astype(jnp.float32)

    def multiply(vector):
        narrow_band_part = vector.astype(jnp.bfloat16)
        ahead_rows = shifted(narrow_band_part[:band_count], "row", -1)
        extended = jnp.concatenate([narrow_band_part, ahead_rows], 0)
        columns = lax.dynamic_slice_in_dim(extended, offset, rows_dev, 0)
        forward = (
            jnp.einsum("kij,kj->ki", blocks, columns, preferred_element_type=jnp.float32)
            * valid_mask
        )
        backward = jnp.einsum(
            "kij,ki->kj", blocks, narrow_band_part, preferred_element_type=jnp.float32
        ) * (valid_mask * upper_mask)
        spread = lax.dynamic_update_slice_in_dim(
            jnp.zeros((rows_dev + band_count, block_size), jnp.float32), backward, offset, 0
        )
        outgoing = narrow_band_part[wanted].astype(jnp.float32)
        far_backward = (
            jnp.einsum(
                "nquo,nqu->nqo",
                distant_local_part,
                narrow_band_part[local_row_values],
                preferred_element_type=jnp.float32,
            )
            * live_mask
        )
        exchanged = lax.all_to_all(
            jnp.concatenate([outgoing, far_backward], 1), "row", split_axis=0, concat_axis=0, tiled=True
        )
        gathered_values = exchanged[:, :slots].astype(jnp.bfloat16)
        returned = exchanged[:, slots:]
        far_forward = (
            jnp.einsum(
                "oqht,oqt->oqh",
                distant_local_part,
                gathered_values,
                preferred_element_type=jnp.float32,
            )
            * live_mask
        )
        summed = forward + spread[:rows_dev]
        summed = summed + jnp.dot(
            pick_in.T, far_forward.reshape(-1, block_size), precision=lax.Precision.HIGHEST
        )
        summed = summed + jnp.dot(
            selection_output.T, returned.reshape(-1, block_size), precision=lax.Precision.HIGHEST
        )
        carried = shifted(spread[rows_dev:], "row", 1)
        summed = jnp.concatenate([summed[:band_count] + carried, summed[band_count:]], 0)
        return all_sum(summed, "band")

    row_sums = multiply(jnp.ones((rows_dev, block_size), jnp.float32))
    scaling = 1.0 / jnp.sqrt(row_sums)
    residual = jnp.zeros_like(scaling)
    for outer_step in range(OUTER):
        balance = scaling * multiply(scaling)
        residual = 1.0 - balance
        scaled = residual / balance
        direction = scaled
        local_product = jnp.sum(residual * scaled)
        growth = jnp.ones_like(scaling)
        for inner_step in range(INNER):
            curved = scaling * multiply(scaling * direction) + balance * direction
            local_curvature = jnp.sum(direction * curved)
            if inner_step == 0:
                totals = all_sum(jnp.stack([local_product, local_curvature]), "row")
                current_residual_product, curvature = totals[0], totals[1]
            else:
                curvature = all_sum(local_curvature[None], "row")[0]
            step_size = current_residual_product / curvature
            growth = growth + step_size * direction
            residual = residual - step_size * curved
            if inner_step + 1 < INNER:
                scaled = residual / balance
                rho_next = all_sum(jnp.sum(residual * scaled)[None], "row")[0]
                direction = scaled + rho_next / current_residual_product * direction
                current_residual_product = rho_next
        scaling = scaling * growth
    return (scaling, residual)


def solution(mesh):
    return jax.shard_map(
        on_device,
        mesh=mesh,
        in_specs=(
            P("row", "band", None, None),
            P("row", "band", None, None, None, None),
            P("row", "band", None, None),
            P("row", "band", None, None),
            P("row", "band", None),
        ),
        out_specs=(P("row", None), P("row", None)),
        check_vma=False,
    )
```

```python
import jax
import jax.numpy as jnp
from jax import lax
from jax.sharding import PartitionSpec as P

OUTER = 2
INNER = 2


def shifted(value, axis, steps):
    count = lax.axis_size(axis)
    leading, last = (max(0, -steps), min(count, count - steps))
    return lax.ppermute(value, axis, [(source, source + steps) for source in range(leading, last)])


def all_sum(value, axis):
    count = lax.axis_size(axis)
    copies = jnp.broadcast_to(value[None], (count,) + value.shape)
    return jnp.sum(lax.all_to_all(copies, axis, 0, 0, tiled=True), 0)


def on_device(band_blocks, distant_block_slots, far_rows, far_columns, far_counts):
    rows_dev = band_blocks.shape[0]
    block_size = band_blocks.shape[2]
    band_count = lax.axis_size("band")
    row_count = lax.axis_size("row")
    offset = lax.axis_index("band")
    row_index = lax.axis_index("row")
    blocks = band_blocks[:, 0]
    distant_local_part = distant_block_slots[0, 0]
    local_row_values = far_rows[0, 0]
    columns_local = far_columns[0, 0]
    counts = far_counts[0, 0]
    slots = local_row_values.shape[1]
    live_mask = (jnp.arange(slots)[None, :] < counts[:, None]).astype(jnp.float32)[..., None]
    block_ids = row_index * rows_dev + jnp.arange(rows_dev)
    valid_mask = (block_ids + offset < row_count * rows_dev).astype(jnp.float32)[:, None]
    upper_mask = (offset > 0).astype(jnp.float32)
    wanted = lax.all_to_all(columns_local, "row", split_axis=0, concat_axis=0, tiled=True)
    targets = jnp.arange(rows_dev)[None, :]
    selection_output = (wanted.reshape(-1)[:, None] == targets).astype(jnp.float32)
    pick_in = (local_row_values.reshape(-1)[:, None] == targets).astype(jnp.float32)

    def multiply(vector):
        narrow_band_part = vector.astype(jnp.bfloat16)
        ahead_rows = shifted(narrow_band_part[:band_count], "row", -1)
        extended = jnp.concatenate([narrow_band_part, ahead_rows], 0)
        columns = lax.dynamic_slice_in_dim(extended, offset, rows_dev, 0)
        forward = (
            jnp.einsum("kij,kj->ki", blocks, columns, preferred_element_type=jnp.float32)
            * valid_mask
        )
        backward = jnp.einsum(
            "kij,ki->kj", blocks, narrow_band_part, preferred_element_type=jnp.float32
        ) * (valid_mask * upper_mask)
        spread = lax.dynamic_update_slice_in_dim(
            jnp.zeros((rows_dev + band_count, block_size), jnp.float32), backward, offset, 0
        )
        outgoing = narrow_band_part[wanted].astype(jnp.float32)
        far_backward = (
            jnp.einsum(
                "nquo,nqu->nqo",
                distant_local_part,
                narrow_band_part[local_row_values],
                preferred_element_type=jnp.float32,
            )
            * live_mask
        )
        exchanged = lax.all_to_all(
            jnp.concatenate([outgoing, far_backward], 1), "row", split_axis=0, concat_axis=0, tiled=True
        )
        gathered_values = exchanged[:, :slots].astype(jnp.bfloat16)
        returned = exchanged[:, slots:]
        far_forward = (
            jnp.einsum(
                "oqht,oqt->oqh",
                distant_local_part,
                gathered_values,
                preferred_element_type=jnp.float32,
            )
            * live_mask
        )
        summed = forward + spread[:rows_dev]
        summed = summed + jnp.dot(
            pick_in.T, far_forward.reshape(-1, block_size), precision=lax.Precision.HIGHEST
        )
        summed = summed + jnp.dot(
            selection_output.T, returned.reshape(-1, block_size), precision=lax.Precision.HIGHEST
        )
        carried = shifted(spread[rows_dev:], "row", 1)
        summed = jnp.concatenate([summed[:band_count] + carried, summed[band_count:]], 0)
        return all_sum(summed, "band")

    row_sums = multiply(jnp.ones((rows_dev, block_size), jnp.float32))
    scaling = 1.0 / jnp.sqrt(row_sums)
    residual = jnp.zeros_like(scaling)
    for outer_step in range(OUTER):
        balance = scaling * multiply(scaling)
        residual = 1.0 - balance
        scaled = residual / balance
        direction = scaled
        local_product = jnp.sum(residual * scaled)
        growth = jnp.ones_like(scaling)
        for inner_step in range(INNER):
            curved = scaling * multiply(scaling * direction) + balance * direction
            last = inner_step + 1 == INNER
            parts = [jnp.sum(direction * curved)]
            if inner_step == 0:
                parts.append(local_product)
            if not last:
                parts.append(jnp.sum(residual * curved / balance))
                parts.append(jnp.sum(curved * curved / balance))
            totals = all_sum(jnp.stack(parts), "row")
            curvature = totals[0]
            if inner_step == 0:
                current_residual_product = totals[1]
            step_size = current_residual_product / curvature
            growth = growth + step_size * direction
            residual = residual - step_size * curved
            if not last:
                cross, square = totals[-2], totals[-1]
                rho_next = current_residual_product - 2.0 * step_size * cross + step_size * step_size * square
                scaled = residual / balance
                direction = scaled + rho_next / current_residual_product * direction
                current_residual_product = rho_next
        scaling = scaling * growth
    return (scaling, residual)


def solution(mesh):
    return jax.shard_map(
        on_device,
        mesh=mesh,
        in_specs=(
            P("row", "band", None, None),
            P("row", "band", None, None, None, None),
            P("row", "band", None, None),
            P("row", "band", None, None),
            P("row", "band", None),
        ),
        out_specs=(P("row", None), P("row", None)),
        check_vma=False,
    )
```

```python
import jax
import jax.numpy as jnp
from jax import lax
from jax.sharding import PartitionSpec as P

OUTER = 2
INNER = 2


def shifted(value, axis, steps):
    count = lax.axis_size(axis)
    leading, last = (max(0, -steps), min(count, count - steps))
    return lax.ppermute(value, axis, [(source, source + steps) for source in range(leading, last)])


def all_sum(value, axis):
    count = lax.axis_size(axis)
    copies = jnp.broadcast_to(value[None], (count,) + value.shape)
    return jnp.sum(lax.all_to_all(copies, axis, 0, 0, tiled=True), 0)


def on_device(band_blocks, distant_block_slots, far_rows, far_columns, far_counts):
    rows_dev = band_blocks.shape[0]
    block_size = band_blocks.shape[2]
    band_count = lax.axis_size("band")
    row_count = lax.axis_size("row")
    offset = lax.axis_index("band")
    row_index = lax.axis_index("row")
    blocks = band_blocks[:, 0]
    distant_local_part = distant_block_slots[0, 0]
    local_row_values = far_rows[0, 0]
    columns_local = far_columns[0, 0]
    counts = far_counts[0, 0]
    slots = local_row_values.shape[1]
    live_mask = (jnp.arange(slots)[None, :] < counts[:, None]).astype(jnp.float32)[..., None]
    block_ids = row_index * rows_dev + jnp.arange(rows_dev)
    valid_mask = (block_ids + offset < row_count * rows_dev).astype(jnp.float32)[:, None]
    upper_mask = (offset > 0).astype(jnp.float32)
    targets = jnp.arange(rows_dev)[None, :]
    pick_in = (local_row_values.reshape(-1)[:, None] == targets).astype(jnp.float32)

    def multiply(vector, wanted=None):
        narrow_band_part = vector.astype(jnp.bfloat16)
        ahead_rows = shifted(narrow_band_part[:band_count], "row", -1)
        extended = jnp.concatenate([narrow_band_part, ahead_rows], 0)
        columns = lax.dynamic_slice_in_dim(extended, offset, rows_dev, 0)
        forward = (
            jnp.einsum("kij,kj->ki", blocks, columns, preferred_element_type=jnp.float32)
            * valid_mask
        )
        backward = jnp.einsum(
            "kij,ki->kj", blocks, narrow_band_part, preferred_element_type=jnp.float32
        ) * (valid_mask * upper_mask)
        spread = lax.dynamic_update_slice_in_dim(
            jnp.zeros((rows_dev + band_count, block_size), jnp.float32), backward, offset, 0
        )
        far_backward = (
            jnp.einsum(
                "nquo,nqu->nqo",
                distant_local_part,
                narrow_band_part[local_row_values],
                preferred_element_type=jnp.float32,
            )
            * live_mask
        )
        if wanted is None:
            column_row = jnp.zeros((row_count, 1, block_size), jnp.float32)
            column_row = column_row.at[:, 0, :slots].set(columns_local.astype(jnp.float32))
            exchanged = lax.all_to_all(
                jnp.concatenate([column_row, far_backward], 1), "row", split_axis=0, concat_axis=0, tiled=True
            )
            wanted = jnp.round(exchanged[:, 0, :slots]).astype(jnp.int32)
            gathered_values = jnp.ones((row_count, slots, block_size), jnp.bfloat16)
            returned = exchanged[:, 1:]
        else:
            outgoing = narrow_band_part[wanted].astype(jnp.float32)
            exchanged = lax.all_to_all(
                jnp.concatenate([outgoing, far_backward], 1), "row", split_axis=0, concat_axis=0, tiled=True
            )
            gathered_values = exchanged[:, :slots].astype(jnp.bfloat16)
            returned = exchanged[:, slots:]
        selection_output = (wanted.reshape(-1)[:, None] == targets).astype(jnp.float32)
        far_forward = (
            jnp.einsum(
                "oqht,oqt->oqh",
                distant_local_part,
                gathered_values,
                preferred_element_type=jnp.float32,
            )
            * live_mask
        )
        summed = forward + spread[:rows_dev]
        summed = summed + jnp.dot(
            pick_in.T, far_forward.reshape(-1, block_size), precision=lax.Precision.HIGHEST
        )
        summed = summed + jnp.dot(
            selection_output.T, returned.reshape(-1, block_size), precision=lax.Precision.HIGHEST
        )
        carried = shifted(spread[rows_dev:], "row", 1)
        summed = jnp.concatenate([summed[:band_count] + carried, summed[band_count:]], 0)
        return all_sum(summed, "band"), wanted

    row_sums, wanted = multiply(jnp.ones((rows_dev, block_size), jnp.float32))
    scaling = 1.0 / jnp.sqrt(row_sums)
    residual = jnp.zeros_like(scaling)
    for outer_step in range(OUTER):
        balance = scaling * multiply(scaling, wanted)[0]
        residual = 1.0 - balance
        scaled = residual / balance
        direction = scaled
        local_product = jnp.sum(residual * scaled)
        growth = jnp.ones_like(scaling)
        for inner_step in range(INNER):
            curved = scaling * multiply(scaling * direction, wanted)[0] + balance * direction
            last = inner_step + 1 == INNER
            parts = [jnp.sum(direction * curved)]
            if inner_step == 0:
                parts.append(local_product)
            if not last:
                parts.append(jnp.sum(residual * curved / balance))
                parts.append(jnp.sum(curved * curved / balance))
            totals = all_sum(jnp.stack(parts), "row")
            curvature = totals[0]
            if inner_step == 0:
                current_residual_product = totals[1]
            step_size = current_residual_product / curvature
            growth = growth + step_size * direction
            residual = residual - step_size * curved
            if not last:
                cross, square = totals[-2], totals[-1]
                rho_next = current_residual_product - 2.0 * step_size * cross + step_size * step_size * square
                scaled = residual / balance
                direction = scaled + rho_next / current_residual_product * direction
                current_residual_product = rho_next
        scaling = scaling * growth
    return (scaling, residual)


def solution(mesh):
    return jax.shard_map(
        on_device,
        mesh=mesh,
        in_specs=(
            P("row", "band", None, None),
            P("row", "band", None, None, None, None),
            P("row", "band", None, None),
            P("row", "band", None, None),
            P("row", "band", None),
        ),
        out_specs=(P("row", None), P("row", None)),
        check_vma=False,
    )
```

```python
import jax
import jax.numpy as jnp
from jax import lax
from jax.sharding import PartitionSpec as P

OUTER = 2
INNER = 2


def shifted(value, axis, steps):
    count = lax.axis_size(axis)
    leading, last = (max(0, -steps), min(count, count - steps))
    return lax.ppermute(value, axis, [(source, source + steps) for source in range(leading, last)])


def all_sum(value, axis):
    count = lax.axis_size(axis)
    copies = jnp.broadcast_to(value[None], (count,) + value.shape)
    return jnp.sum(lax.all_to_all(copies, axis, 0, 0, tiled=True), 0)


def combine(parts, coefficients):
    total = parts[0] if coefficients[0] is None else coefficients[0] * parts[0]
    for index in range(1, len(coefficients)):
        total = total + coefficients[index] * parts[index]
    return total


def on_device(band_blocks, distant_block_slots, far_rows, far_columns, far_counts):
    rows_dev = band_blocks.shape[0]
    block_size = band_blocks.shape[2]
    band_count = lax.axis_size("band")
    row_count = lax.axis_size("row")
    offset = lax.axis_index("band")
    row_index = lax.axis_index("row")
    blocks = band_blocks[:, 0]
    distant_local_part = distant_block_slots[0, 0]
    local_row_values = far_rows[0, 0]
    columns_local = far_columns[0, 0]
    counts = far_counts[0, 0]
    slots = local_row_values.shape[1]
    live_mask = (jnp.arange(slots)[None, :] < counts[:, None]).astype(jnp.float32)[..., None]
    block_ids = row_index * rows_dev + jnp.arange(rows_dev)
    valid_mask = (block_ids + offset < row_count * rows_dev).astype(jnp.float32)[:, None]
    upper_mask = (offset > 0).astype(jnp.float32)
    targets = jnp.arange(rows_dev)[None, :]
    pick_in = (local_row_values.reshape(-1)[:, None] == targets).astype(jnp.float32)
    wide_blocks = blocks.astype(jnp.float32)
    wide_distant = distant_local_part.astype(jnp.float32)

    def band_backward(vector, wide):
        if wide:
            product = jnp.einsum(
                "kij,ki->kj", wide_blocks, vector, precision=lax.Precision.HIGHEST
            )
        else:
            product = jnp.einsum(
                "kij,ki->kj", blocks, vector, preferred_element_type=jnp.float32
            )
        product = product * (valid_mask * upper_mask)
        return lax.dynamic_update_slice_in_dim(
            jnp.zeros((rows_dev + band_count, block_size), jnp.float32), product, offset, 0
        )

    def far_transposed(vector, wide):
        if wide:
            product = jnp.einsum(
                "nquo,nqu->nqo",
                wide_distant,
                vector[local_row_values],
                precision=lax.Precision.HIGHEST,
            )
        else:
            product = jnp.einsum(
                "nquo,nqu->nqo",
                distant_local_part,
                vector[local_row_values],
                preferred_element_type=jnp.float32,
            )
        return product * live_mask

    def finish(narrow_band_part, ahead_rows, spread, gathered_values, returned, carried, wanted):
        extended = jnp.concatenate([narrow_band_part, ahead_rows], 0)
        columns = lax.dynamic_slice_in_dim(extended, offset, rows_dev, 0)
        forward = (
            jnp.einsum("kij,kj->ki", blocks, columns, preferred_element_type=jnp.float32)
            * valid_mask
        )
        far_forward = (
            jnp.einsum(
                "oqht,oqt->oqh",
                distant_local_part,
                gathered_values,
                preferred_element_type=jnp.float32,
            )
            * live_mask
        )
        selection_output = (wanted.reshape(-1)[:, None] == targets).astype(jnp.float32)
        summed = forward + spread[:rows_dev]
        summed = summed + jnp.dot(
            pick_in.T, far_forward.reshape(-1, block_size), precision=lax.Precision.HIGHEST
        )
        summed = summed + jnp.dot(
            selection_output.T, returned.reshape(-1, block_size), precision=lax.Precision.HIGHEST
        )
        summed = jnp.concatenate([summed[:band_count] + carried, summed[band_count:]], 0)
        return all_sum(summed, "band")

    def multiply(vector, wanted=None):
        narrow_band_part = vector.astype(jnp.bfloat16)
        ahead_rows = shifted(narrow_band_part[:band_count], "row", -1)
        spread = band_backward(narrow_band_part, False)
        far_backward = far_transposed(narrow_band_part, False)
        if wanted is None:
            column_row = jnp.zeros((row_count, 1, block_size), jnp.float32)
            column_row = column_row.at[:, 0, :slots].set(columns_local.astype(jnp.float32))
            exchanged = lax.all_to_all(
                jnp.concatenate([column_row, far_backward], 1), "row", split_axis=0, concat_axis=0, tiled=True
            )
            wanted = jnp.round(exchanged[:, 0, :slots]).astype(jnp.int32)
            gathered_values = jnp.ones((row_count, slots, block_size), jnp.bfloat16)
            returned = exchanged[:, 1:]
        else:
            outgoing = narrow_band_part[wanted].astype(jnp.float32)
            exchanged = lax.all_to_all(
                jnp.concatenate([outgoing, far_backward], 1), "row", split_axis=0, concat_axis=0, tiled=True
            )
            gathered_values = exchanged[:, :slots].astype(jnp.bfloat16)
            returned = exchanged[:, slots:]
        carried = shifted(spread[rows_dev:], "row", 1)
        result = finish(narrow_band_part, ahead_rows, spread, gathered_values, returned, carried, wanted)
        return result, wanted

    def multiply_pending(parts, partials, coefficients_of, wanted):
        count = len(parts)
        stacked = jnp.stack(parts)
        ahead_parts = shifted(stacked[:, :band_count], "row", -1)
        carried_parts = shifted(
            jnp.stack([band_backward(part, True)[rows_dev:] for part in parts]), "row", 1
        )
        outgoing = jnp.concatenate([part[wanted] for part in parts], 1)
        far_backward = jnp.concatenate([far_transposed(part, True) for part in parts], 1)
        scalar_row = jnp.zeros((row_count, 1, block_size), jnp.float32)
        scalar_row = scalar_row.at[:, 0, : partials.shape[0]].set(
            jnp.broadcast_to(partials[None], (row_count, partials.shape[0]))
        )
        exchanged = lax.all_to_all(
            jnp.concatenate([outgoing, far_backward, scalar_row], 1),
            "row",
            split_axis=0,
            concat_axis=0,
            tiled=True,
        )
        totals = jnp.sum(exchanged[:, count * 2 * slots, : partials.shape[0]], 0)
        coefficients = coefficients_of(totals)
        narrow_band_part = combine(parts, coefficients).astype(jnp.bfloat16)
        ahead_rows = combine(list(ahead_parts), coefficients).astype(jnp.bfloat16)
        spread = band_backward(narrow_band_part, False)
        gathered_values = combine(
            [exchanged[:, index * slots : (index + 1) * slots] for index in range(count)], coefficients
        ).astype(jnp.bfloat16)
        returned = combine(
            [
                exchanged[:, (count + index) * slots : (count + index + 1) * slots]
                for index in range(count)
            ],
            coefficients,
        )
        carried = combine(list(carried_parts), coefficients)
        result = finish(narrow_band_part, ahead_rows, spread, gathered_values, returned, carried, wanted)
        return result, totals

    row_sums, wanted = multiply(jnp.ones((rows_dev, block_size), jnp.float32))
    scaling = 1.0 / jnp.sqrt(row_sums)
    residual = jnp.zeros_like(scaling)
    pending = None
    for outer_step in range(OUTER):
        if pending is None:
            product = multiply(scaling, wanted)[0]
        else:
            growth, direction, curved, current_residual_product, local_curvature = pending

            def boundary_coefficients(totals, rho=current_residual_product):
                return [None, rho / totals[0]]

            product, totals = multiply_pending(
                [scaling * growth, scaling * direction],
                local_curvature[None],
                boundary_coefficients,
                wanted,
            )
            step_size = current_residual_product / totals[0]
            growth = growth + step_size * direction
            residual = residual - step_size * curved
            scaling = scaling * growth
            pending = None
        balance = scaling * product
        residual = 1.0 - balance
        scaled = residual / balance
        direction = scaled
        local_product = jnp.sum(residual * scaled)
        growth = jnp.ones_like(scaling)
        curved = scaling * multiply(scaling * direction, wanted)[0] + balance * direction
        partials = jnp.stack(
            [
                jnp.sum(direction * curved),
                local_product,
                jnp.sum(residual * curved / balance),
                jnp.sum(curved * curved / balance),
            ]
        )
        current_residual_product = None
        for inner_step in range(1, INNER):

            def inner_coefficients(totals, rho=current_residual_product):
                if rho is None:
                    rho = totals[1]
                step = rho / totals[0]
                rho_next = rho - 2.0 * step * totals[2] + step * step * totals[3]
                return [None, -step, rho_next / rho]

            product, totals = multiply_pending(
                [scaling * residual / balance, scaling * curved / balance, scaling * direction],
                partials,
                inner_coefficients,
                wanted,
            )
            if current_residual_product is None:
                current_residual_product = totals[1]
            curvature = totals[0]
            step_size = current_residual_product / curvature
            growth = growth + step_size * direction
            residual = residual - step_size * curved
            rho_next = (
                current_residual_product
                - 2.0 * step_size * totals[2]
                + step_size * step_size * totals[3]
            )
            scaled = residual / balance
            direction = scaled + rho_next / current_residual_product * direction
            current_residual_product = rho_next
            curved = scaling * product + balance * direction
            partials = jnp.stack(
                [
                    jnp.sum(direction * curved),
                    jnp.zeros_like(rho_next),
                    jnp.sum(residual * curved / balance),
                    jnp.sum(curved * curved / balance),
                ]
            )
        if outer_step + 1 < OUTER:
            pending = (growth, direction, curved, current_residual_product, partials[0])
        else:
            curvature = all_sum(partials[0][None], "row")[0]
            step_size = current_residual_product / curvature
            growth = growth + step_size * direction
            residual = residual - step_size * curved
            scaling = scaling * growth
    return (scaling, residual)


def solution(mesh):
    return jax.shard_map(
        on_device,
        mesh=mesh,
        in_specs=(
            P("row", "band", None, None),
            P("row", "band", None, None, None, None),
            P("row", "band", None, None),
            P("row", "band", None, None),
            P("row", "band", None),
        ),
        out_specs=(P("row", None), P("row", None)),
        check_vma=False,
    )
```

```python
import jax
import jax.numpy as jnp
from jax import lax
from jax.sharding import PartitionSpec as P

OUTER = 2
INNER = 2


def shifted(value, axis, steps):
    count = lax.axis_size(axis)
    leading, last = (max(0, -steps), min(count, count - steps))
    return lax.ppermute(value, axis, [(source, source + steps) for source in range(leading, last)])


def all_sum(value, axis):
    count = lax.axis_size(axis)
    copies = jnp.broadcast_to(value[None], (count,) + value.shape)
    return jnp.sum(lax.all_to_all(copies, axis, 0, 0, tiled=True), 0)


def on_device(band_blocks, distant_block_slots, far_rows, far_columns, far_counts):
    rows_dev = band_blocks.shape[0]
    block_size = band_blocks.shape[2]
    band_count = lax.axis_size("band")
    row_count = lax.axis_size("row")
    offset = lax.axis_index("band")
    row_index = lax.axis_index("row")
    blocks = band_blocks[:, 0]
    distant_local_part = distant_block_slots[0, 0]
    local_row_values = far_rows[0, 0]
    columns_local = far_columns[0, 0]
    counts = far_counts[0, 0]
    slots = local_row_values.shape[1]
    live_mask = (jnp.arange(slots)[None, :] < counts[:, None]).astype(jnp.float32)[..., None]
    block_ids = row_index * rows_dev + jnp.arange(rows_dev)
    valid_mask = (block_ids + offset < row_count * rows_dev).astype(jnp.float32)[:, None]
    upper_mask = (offset > 0).astype(jnp.float32)
    targets = jnp.arange(rows_dev)[None, :]
    pick_in = (local_row_values.reshape(-1)[:, None] == targets).astype(jnp.float32)

    def multiply(vector, wanted=None):
        narrow_band_part = vector.astype(jnp.bfloat16)
        ahead_rows = shifted(narrow_band_part[:band_count], "row", -1)
        extended = jnp.concatenate([narrow_band_part, ahead_rows], 0)
        columns = lax.dynamic_slice_in_dim(extended, offset, rows_dev, 0)
        forward = (
            jnp.einsum("kij,kj->ki", blocks, columns, preferred_element_type=jnp.float32)
            * valid_mask
        )
        backward = jnp.einsum(
            "kij,ki->kj", blocks, narrow_band_part, preferred_element_type=jnp.float32
        ) * (valid_mask * upper_mask)
        spread = lax.dynamic_update_slice_in_dim(
            jnp.zeros((rows_dev + band_count, block_size), jnp.float32), backward, offset, 0
        )
        far_backward = (
            jnp.einsum(
                "nquo,nqu->nqo",
                distant_local_part,
                narrow_band_part[local_row_values],
                preferred_element_type=jnp.float32,
            )
            * live_mask
        )
        if wanted is None:
            column_row = jnp.zeros((row_count, 1, block_size), jnp.float32)
            column_row = column_row.at[:, 0, :slots].set(columns_local.astype(jnp.float32))
            exchanged = lax.all_to_all(
                jnp.concatenate([column_row, far_backward], 1), "row", split_axis=0, concat_axis=0, tiled=True
            )
            wanted = jnp.round(exchanged[:, 0, :slots]).astype(jnp.int32)
            gathered_values = jnp.ones((row_count, slots, block_size), jnp.bfloat16)
            returned = exchanged[:, 1:]
        else:
            outgoing = narrow_band_part[wanted].astype(jnp.float32)
            exchanged = lax.all_to_all(
                jnp.concatenate([outgoing, far_backward], 1), "row", split_axis=0, concat_axis=0, tiled=True
            )
            gathered_values = exchanged[:, :slots].astype(jnp.bfloat16)
            returned = exchanged[:, slots:]
        selection_output = (wanted.reshape(-1)[:, None] == targets).astype(jnp.float32)
        far_forward = (
            jnp.einsum(
                "oqht,oqt->oqh",
                distant_local_part,
                gathered_values,
                preferred_element_type=jnp.float32,
            )
            * live_mask
        )
        summed = forward + spread[:rows_dev]
        summed = summed + jnp.dot(
            pick_in.T, far_forward.reshape(-1, block_size), precision=lax.Precision.HIGHEST
        )
        summed = summed + jnp.dot(
            selection_output.T, returned.reshape(-1, block_size), precision=lax.Precision.HIGHEST
        )
        carried = shifted(spread[rows_dev:], "row", 1)
        summed = jnp.concatenate([summed[:band_count] + carried, summed[band_count:]], 0)
        return all_sum(summed, "band"), wanted

    row_sums, wanted = multiply(jnp.ones((rows_dev, block_size), jnp.float32))
    scaling = 1.0 / jnp.sqrt(row_sums)
    residual = jnp.zeros_like(scaling)
    for outer_step in range(OUTER):
        balance = scaling * multiply(scaling, wanted)[0]
        residual = 1.0 - balance
        scaled = residual / balance
        direction = scaled
        local_product = residual * scaled
        growth = jnp.ones_like(scaling)
        for inner_step in range(INNER):
            curved = scaling * multiply(scaling * direction, wanted)[0] + balance * direction
            last = inner_step + 1 == INNER
            parts = [direction * curved]
            if inner_step == 0:
                parts.append(local_product)
            if not last:
                parts.append(residual * curved / balance)
                parts.append(curved * curved / balance)
            stacked = jnp.stack(parts).reshape(len(parts), -1)
            local_totals = jnp.dot(
                stacked, jnp.ones((stacked.shape[1],), jnp.float32), precision=lax.Precision.HIGHEST
            )
            totals = all_sum(local_totals, "row")
            curvature = totals[0]
            if inner_step == 0:
                current_residual_product = totals[1]
            step_size = current_residual_product / curvature
            growth = growth + step_size * direction
            residual = residual - step_size * curved
            if not last:
                cross, square = totals[-2], totals[-1]
                rho_next = current_residual_product - 2.0 * step_size * cross + step_size * step_size * square
                scaled = residual / balance
                direction = scaled + rho_next / current_residual_product * direction
                current_residual_product = rho_next
        scaling = scaling * growth
    return (scaling, residual)


def solution(mesh):
    return jax.shard_map(
        on_device,
        mesh=mesh,
        in_specs=(
            P("row", "band", None, None),
            P("row", "band", None, None, None, None),
            P("row", "band", None, None),
            P("row", "band", None, None),
            P("row", "band", None),
        ),
        out_specs=(P("row", None), P("row", None)),
        check_vma=False,
    )
```

```python
import jax
import jax.numpy as jnp
from jax import lax
from jax.sharding import PartitionSpec as P

OUTER = 2
INNER = 2


def shifted(value, axis, steps):
    count = lax.axis_size(axis)
    leading, last = (max(0, -steps), min(count, count - steps))
    return lax.ppermute(value, axis, [(source, source + steps) for source in range(leading, last)])


def all_sum(value, axis):
    count = lax.axis_size(axis)
    copies = jnp.broadcast_to(value[None], (count,) + value.shape)
    return jnp.sum(lax.all_to_all(copies, axis, 0, 0, tiled=True), 0)


def lane_totals(value, axis, lanes):
    count = lax.axis_size(axis)
    copies = jnp.broadcast_to(value[None], (count,) + value.shape)
    received = lax.all_to_all(copies, axis, 0, 0, tiled=True)
    return jnp.dot(received.T, jnp.ones((count, lanes), jnp.float32), precision=lax.Precision.HIGHEST)


def on_device(band_blocks, distant_block_slots, far_rows, far_columns, far_counts):
    rows_dev = band_blocks.shape[0]
    block_size = band_blocks.shape[2]
    band_count = lax.axis_size("band")
    row_count = lax.axis_size("row")
    offset = lax.axis_index("band")
    row_index = lax.axis_index("row")
    blocks = band_blocks[:, 0]
    distant_local_part = distant_block_slots[0, 0]
    local_row_values = far_rows[0, 0]
    columns_local = far_columns[0, 0]
    counts = far_counts[0, 0]
    slots = local_row_values.shape[1]
    live_mask = (jnp.arange(slots)[None, :] < counts[:, None]).astype(jnp.float32)[..., None]
    block_ids = row_index * rows_dev + jnp.arange(rows_dev)
    valid_mask = (block_ids + offset < row_count * rows_dev).astype(jnp.float32)[:, None]
    upper_mask = (offset > 0).astype(jnp.float32)
    targets = jnp.arange(rows_dev)[None, :]
    pick_in = (local_row_values.reshape(-1)[:, None] == targets).astype(jnp.float32)

    def multiply(vector, wanted=None):
        narrow_band_part = vector.astype(jnp.bfloat16)
        ahead_rows = shifted(narrow_band_part[:band_count], "row", -1)
        extended = jnp.concatenate([narrow_band_part, ahead_rows], 0)
        columns = lax.dynamic_slice_in_dim(extended, offset, rows_dev, 0)
        forward = (
            jnp.einsum("kij,kj->ki", blocks, columns, preferred_element_type=jnp.float32)
            * valid_mask
        )
        backward = jnp.einsum(
            "kij,ki->kj", blocks, narrow_band_part, preferred_element_type=jnp.float32
        ) * (valid_mask * upper_mask)
        spread = lax.dynamic_update_slice_in_dim(
            jnp.zeros((rows_dev + band_count, block_size), jnp.float32), backward, offset, 0
        )
        far_backward = (
            jnp.einsum(
                "nquo,nqu->nqo",
                distant_local_part,
                narrow_band_part[local_row_values],
                preferred_element_type=jnp.float32,
            )
            * live_mask
        )
        if wanted is None:
            column_row = jnp.zeros((row_count, 1, block_size), jnp.float32)
            column_row = column_row.at[:, 0, :slots].set(columns_local.astype(jnp.float32))
            exchanged = lax.all_to_all(
                jnp.concatenate([column_row, far_backward], 1), "row", split_axis=0, concat_axis=0, tiled=True
            )
            wanted = jnp.round(exchanged[:, 0, :slots]).astype(jnp.int32)
            gathered_values = jnp.ones((row_count, slots, block_size), jnp.bfloat16)
            returned = exchanged[:, 1:]
        else:
            outgoing = narrow_band_part[wanted].astype(jnp.float32)
            exchanged = lax.all_to_all(
                jnp.concatenate([outgoing, far_backward], 1), "row", split_axis=0, concat_axis=0, tiled=True
            )
            gathered_values = exchanged[:, :slots].astype(jnp.bfloat16)
            returned = exchanged[:, slots:]
        selection_output = (wanted.reshape(-1)[:, None] == targets).astype(jnp.float32)
        far_forward = (
            jnp.einsum(
                "oqht,oqt->oqh",
                distant_local_part,
                gathered_values,
                preferred_element_type=jnp.float32,
            )
            * live_mask
        )
        summed = forward + spread[:rows_dev]
        summed = summed + jnp.dot(
            pick_in.T, far_forward.reshape(-1, block_size), precision=lax.Precision.HIGHEST
        )
        summed = summed + jnp.dot(
            selection_output.T, returned.reshape(-1, block_size), precision=lax.Precision.HIGHEST
        )
        carried = shifted(spread[rows_dev:], "row", 1)
        summed = jnp.concatenate([summed[:band_count] + carried, summed[band_count:]], 0)
        return all_sum(summed, "band"), wanted

    row_sums, wanted = multiply(jnp.ones((rows_dev, block_size), jnp.float32))
    scaling = 1.0 / jnp.sqrt(row_sums)
    residual = jnp.zeros_like(scaling)
    for outer_step in range(OUTER):
        balance = scaling * multiply(scaling, wanted)[0]
        residual = 1.0 - balance
        scaled = residual / balance
        direction = scaled
        local_product = residual * scaled
        growth = jnp.ones_like(scaling)
        for inner_step in range(INNER):
            curved = scaling * multiply(scaling * direction, wanted)[0] + balance * direction
            last = inner_step + 1 == INNER
            parts = [direction * curved]
            if inner_step == 0:
                parts.append(local_product)
            if not last:
                parts.append(residual * curved / balance)
                parts.append(curved * curved / balance)
            stacked = jnp.stack(parts).reshape(len(parts), -1)
            local_totals = jnp.dot(
                stacked, jnp.ones((stacked.shape[1],), jnp.float32), precision=lax.Precision.HIGHEST
            )
            totals = lane_totals(local_totals, "row", block_size)
            curvature = totals[0]
            if inner_step == 0:
                current_residual_product = totals[1]
            step_size = current_residual_product / curvature
            growth = growth + step_size * direction
            residual = residual - step_size * curved
            if not last:
                cross, square = totals[-2], totals[-1]
                rho_next = current_residual_product - 2.0 * step_size * cross + step_size * step_size * square
                scaled = residual / balance
                direction = scaled + rho_next / current_residual_product * direction
                current_residual_product = rho_next
        scaling = scaling * growth
    return (scaling, residual)


def solution(mesh):
    return jax.shard_map(
        on_device,
        mesh=mesh,
        in_specs=(
            P("row", "band", None, None),
            P("row", "band", None, None, None, None),
            P("row", "band", None, None),
            P("row", "band", None, None),
            P("row", "band", None),
        ),
        out_specs=(P("row", None), P("row", None)),
        check_vma=False,
    )
```

```python
import jax
import jax.numpy as jnp
from jax import lax
from jax.sharding import PartitionSpec as P

OUTER = 2
INNER = 2


def shifted(value, axis, steps):
    count = lax.axis_size(axis)
    leading, last = (max(0, -steps), min(count, count - steps))
    return lax.ppermute(value, axis, [(source, source + steps) for source in range(leading, last)])


def all_sum(value, axis):
    count = lax.axis_size(axis)
    copies = jnp.broadcast_to(value[None], (count,) + value.shape)
    return jnp.sum(lax.all_to_all(copies, axis, 0, 0, tiled=True), 0)


def lane_totals(value, axis, lanes):
    count = lax.axis_size(axis)
    copies = jnp.broadcast_to(value[None], (count,) + value.shape)
    received = lax.all_to_all(copies, axis, 0, 0, tiled=True)
    return jnp.dot(received.T, jnp.ones((count, lanes), jnp.float32), precision=lax.Precision.HIGHEST)


def on_device(band_blocks, distant_block_slots, far_rows, far_columns, far_counts):
    rows_dev = band_blocks.shape[0]
    block_size = band_blocks.shape[2]
    band_count = lax.axis_size("band")
    row_count = lax.axis_size("row")
    offset = lax.axis_index("band")
    row_index = lax.axis_index("row")
    blocks = band_blocks[:, 0]
    distant_local_part = distant_block_slots[0, 0]
    local_row_values = far_rows[0, 0]
    columns_local = far_columns[0, 0]
    counts = far_counts[0, 0]
    slots = local_row_values.shape[1]
    live_mask = (jnp.arange(slots)[None, :] < counts[:, None]).astype(jnp.float32)[..., None]
    block_ids = row_index * rows_dev + jnp.arange(rows_dev)
    valid_mask = (block_ids + offset < row_count * rows_dev).astype(jnp.float32)[:, None]
    upper_mask = (offset > 0).astype(jnp.float32)
    targets = jnp.arange(rows_dev)[None, :]
    pick_in = (local_row_values.reshape(-1)[:, None] == targets).astype(jnp.float32)
    pick_rows = pick_in.astype(jnp.bfloat16)

    def picked(selection, vector):
        product = jnp.dot(selection, vector, preferred_element_type=jnp.float32)
        return product.reshape(row_count, slots, block_size)

    def multiply(vector, wanted=None):
        narrow_band_part = vector.astype(jnp.bfloat16)
        ahead_rows = shifted(narrow_band_part[:band_count], "row", -1)
        extended = jnp.concatenate([narrow_band_part, ahead_rows], 0)
        columns = lax.dynamic_slice_in_dim(extended, offset, rows_dev, 0)
        forward = (
            jnp.einsum("kij,kj->ki", blocks, columns, preferred_element_type=jnp.float32)
            * valid_mask
        )
        backward = jnp.einsum(
            "kij,ki->kj", blocks, narrow_band_part, preferred_element_type=jnp.float32
        ) * (valid_mask * upper_mask)
        spread = lax.dynamic_update_slice_in_dim(
            jnp.zeros((rows_dev + band_count, block_size), jnp.float32), backward, offset, 0
        )
        far_backward = (
            jnp.einsum(
                "nquo,nqu->nqo",
                distant_local_part,
                picked(pick_rows, narrow_band_part).astype(jnp.bfloat16),
                preferred_element_type=jnp.float32,
            )
            * live_mask
        )
        if wanted is None:
            column_row = jnp.zeros((row_count, 1, block_size), jnp.float32)
            column_row = column_row.at[:, 0, :slots].set(columns_local.astype(jnp.float32))
            exchanged = lax.all_to_all(
                jnp.concatenate([column_row, far_backward], 1), "row", split_axis=0, concat_axis=0, tiled=True
            )
            wanted = jnp.round(exchanged[:, 0, :slots]).astype(jnp.int32)
            gathered_values = jnp.ones((row_count, slots, block_size), jnp.bfloat16)
            returned = exchanged[:, 1:]
        else:
            pick_out = (wanted.reshape(-1)[:, None] == targets).astype(jnp.bfloat16)
            outgoing = picked(pick_out, narrow_band_part)
            exchanged = lax.all_to_all(
                jnp.concatenate([outgoing, far_backward], 1), "row", split_axis=0, concat_axis=0, tiled=True
            )
            gathered_values = exchanged[:, :slots].astype(jnp.bfloat16)
            returned = exchanged[:, slots:]
        selection_output = (wanted.reshape(-1)[:, None] == targets).astype(jnp.float32)
        far_forward = (
            jnp.einsum(
                "oqht,oqt->oqh",
                distant_local_part,
                gathered_values,
                preferred_element_type=jnp.float32,
            )
            * live_mask
        )
        summed = forward + spread[:rows_dev]
        summed = summed + jnp.dot(
            pick_in.T, far_forward.reshape(-1, block_size), precision=lax.Precision.HIGHEST
        )
        summed = summed + jnp.dot(
            selection_output.T, returned.reshape(-1, block_size), precision=lax.Precision.HIGHEST
        )
        carried = shifted(spread[rows_dev:], "row", 1)
        summed = jnp.concatenate([summed[:band_count] + carried, summed[band_count:]], 0)
        return all_sum(summed, "band"), wanted

    row_sums, wanted = multiply(jnp.ones((rows_dev, block_size), jnp.float32))
    scaling = 1.0 / jnp.sqrt(row_sums)
    residual = jnp.zeros_like(scaling)
    for outer_step in range(OUTER):
        balance = scaling * multiply(scaling, wanted)[0]
        residual = 1.0 - balance
        scaled = residual / balance
        direction = scaled
        local_product = residual * scaled
        growth = jnp.ones_like(scaling)
        for inner_step in range(INNER):
            curved = scaling * multiply(scaling * direction, wanted)[0] + balance * direction
            last = inner_step + 1 == INNER
            parts = [direction * curved]
            if inner_step == 0:
                parts.append(local_product)
            if not last:
                parts.append(residual * curved / balance)
                parts.append(curved * curved / balance)
            stacked = jnp.stack(parts).reshape(len(parts), -1)
            local_totals = jnp.dot(
                stacked, jnp.ones((stacked.shape[1],), jnp.float32), precision=lax.Precision.HIGHEST
            )
            totals = lane_totals(local_totals, "row", block_size)
            curvature = totals[0]
            if inner_step == 0:
                current_residual_product = totals[1]
            step_size = current_residual_product / curvature
            growth = growth + step_size * direction
            residual = residual - step_size * curved
            if not last:
                cross, square = totals[-2], totals[-1]
                rho_next = current_residual_product - 2.0 * step_size * cross + step_size * step_size * square
                scaled = residual / balance
                direction = scaled + rho_next / current_residual_product * direction
                current_residual_product = rho_next
        scaling = scaling * growth
    return (scaling, residual)


def solution(mesh):
    return jax.shard_map(
        on_device,
        mesh=mesh,
        in_specs=(
            P("row", "band", None, None),
            P("row", "band", None, None, None, None),
            P("row", "band", None, None),
            P("row", "band", None, None),
            P("row", "band", None),
        ),
        out_specs=(P("row", None), P("row", None)),
        check_vma=False,
    )
```

```python
import jax
import jax.numpy as jnp
from jax import lax
from jax.sharding import PartitionSpec as P

OUTER = 2
INNER = 2


def shifted(value, axis, steps):
    count = lax.axis_size(axis)
    leading, last = (max(0, -steps), min(count, count - steps))
    return lax.ppermute(value, axis, [(source, source + steps) for source in range(leading, last)])


def all_sum(value, axis):
    count = lax.axis_size(axis)
    copies = jnp.broadcast_to(value[None], (count,) + value.shape)
    return jnp.sum(lax.all_to_all(copies, axis, 0, 0, tiled=True), 0)


def lane_totals(copies, axis, lanes):
    count = lax.axis_size(axis)
    received = lax.all_to_all(copies, axis, 0, 0, tiled=True)
    return jnp.dot(received.T, jnp.ones((count, lanes), jnp.float32), precision=lax.Precision.HIGHEST)


def on_device(band_blocks, distant_block_slots, far_rows, far_columns, far_counts):
    rows_dev = band_blocks.shape[0]
    block_size = band_blocks.shape[2]
    band_count = lax.axis_size("band")
    row_count = lax.axis_size("row")
    offset = lax.axis_index("band")
    row_index = lax.axis_index("row")
    blocks = band_blocks[:, 0]
    distant_local_part = distant_block_slots[0, 0]
    local_row_values = far_rows[0, 0]
    columns_local = far_columns[0, 0]
    counts = far_counts[0, 0]
    slots = local_row_values.shape[1]
    live_mask = (jnp.arange(slots)[None, :] < counts[:, None]).astype(jnp.float32)[..., None]
    block_ids = row_index * rows_dev + jnp.arange(rows_dev)
    valid_mask = (block_ids + offset < row_count * rows_dev).astype(jnp.float32)[:, None]
    upper_mask = (offset > 0).astype(jnp.float32)
    targets = jnp.arange(rows_dev)[None, :]
    pick_in = (local_row_values.reshape(-1)[:, None] == targets).astype(jnp.float32)
    pick_rows = pick_in.astype(jnp.bfloat16)

    def picked(selection, vector):
        product = jnp.dot(selection, vector, preferred_element_type=jnp.float32)
        return product.reshape(row_count, slots, block_size)

    def multiply(vector, wanted=None):
        narrow_band_part = vector.astype(jnp.bfloat16)
        ahead_rows = shifted(narrow_band_part[:band_count], "row", -1)
        extended = jnp.concatenate([narrow_band_part, ahead_rows], 0)
        columns = lax.dynamic_slice_in_dim(extended, offset, rows_dev, 0)
        forward = (
            jnp.einsum("kij,kj->ki", blocks, columns, preferred_element_type=jnp.float32)
            * valid_mask
        )
        backward = jnp.einsum(
            "kij,ki->kj", blocks, narrow_band_part, preferred_element_type=jnp.float32
        ) * (valid_mask * upper_mask)
        spread = lax.dynamic_update_slice_in_dim(
            jnp.zeros((rows_dev + band_count, block_size), jnp.float32), backward, offset, 0
        )
        far_backward = (
            jnp.einsum(
                "nquo,nqu->nqo",
                distant_local_part,
                picked(pick_rows, narrow_band_part).astype(jnp.bfloat16),
                preferred_element_type=jnp.float32,
            )
            * live_mask
        )
        if wanted is None:
            column_row = jnp.zeros((row_count, 1, block_size), jnp.float32)
            column_row = column_row.at[:, 0, :slots].set(columns_local.astype(jnp.float32))
            exchanged = lax.all_to_all(
                jnp.concatenate([column_row, far_backward], 1), "row", split_axis=0, concat_axis=0, tiled=True
            )
            wanted = jnp.round(exchanged[:, 0, :slots]).astype(jnp.int32)
            gathered_values = jnp.ones((row_count, slots, block_size), jnp.bfloat16)
            returned = exchanged[:, 1:]
        else:
            pick_out = (wanted.reshape(-1)[:, None] == targets).astype(jnp.bfloat16)
            outgoing = picked(pick_out, narrow_band_part)
            exchanged = lax.all_to_all(
                jnp.concatenate([outgoing, far_backward], 1), "row", split_axis=0, concat_axis=0, tiled=True
            )
            gathered_values = exchanged[:, :slots].astype(jnp.bfloat16)
            returned = exchanged[:, slots:]
        selection_output = (wanted.reshape(-1)[:, None] == targets).astype(jnp.float32)
        far_forward = (
            jnp.einsum(
                "oqht,oqt->oqh",
                distant_local_part,
                gathered_values,
                preferred_element_type=jnp.float32,
            )
            * live_mask
        )
        summed = forward + spread[:rows_dev]
        summed = summed + jnp.dot(
            pick_in.T, far_forward.reshape(-1, block_size), precision=lax.Precision.HIGHEST
        )
        summed = summed + jnp.dot(
            selection_output.T, returned.reshape(-1, block_size), precision=lax.Precision.HIGHEST
        )
        carried = shifted(spread[rows_dev:], "row", 1)
        summed = jnp.concatenate([summed[:band_count] + carried, summed[band_count:]], 0)
        return all_sum(summed, "band"), wanted

    row_sums, wanted = multiply(jnp.ones((rows_dev, block_size), jnp.float32))
    scaling = 1.0 / jnp.sqrt(row_sums)
    residual = jnp.zeros_like(scaling)
    for outer_step in range(OUTER):
        balance = scaling * multiply(scaling, wanted)[0]
        residual = 1.0 - balance
        scaled = residual / balance
        direction = scaled
        local_product = residual * scaled
        growth = jnp.ones_like(scaling)
        for inner_step in range(INNER):
            curved = scaling * multiply(scaling * direction, wanted)[0] + balance * direction
            last = inner_step + 1 == INNER
            parts = [direction * curved]
            if inner_step == 0:
                parts.append(local_product)
            if not last:
                parts.append(residual * curved / balance)
                parts.append(curved * curved / balance)
            stacked = jnp.stack(parts).reshape(len(parts), -1)
            copies = jnp.dot(
                jnp.ones((row_count, stacked.shape[1]), jnp.float32), stacked.T, precision=lax.Precision.HIGHEST
            )
            totals = lane_totals(copies, "row", block_size)
            curvature = totals[0]
            if inner_step == 0:
                current_residual_product = totals[1]
            step_size = current_residual_product / curvature
            growth = growth + step_size * direction
            residual = residual - step_size * curved
            if not last:
                cross, square = totals[-2], totals[-1]
                rho_next = current_residual_product - 2.0 * step_size * cross + step_size * step_size * square
                scaled = residual / balance
                direction = scaled + rho_next / current_residual_product * direction
                current_residual_product = rho_next
        scaling = scaling * growth
    return (scaling, residual)


def solution(mesh):
    return jax.shard_map(
        on_device,
        mesh=mesh,
        in_specs=(
            P("row", "band", None, None),
            P("row", "band", None, None, None, None),
            P("row", "band", None, None),
            P("row", "band", None, None),
            P("row", "band", None),
        ),
        out_specs=(P("row", None), P("row", None)),
        check_vma=False,
    )
```

```python
import jax
import jax.numpy as jnp
from jax import lax
from jax.sharding import PartitionSpec as P

OUTER = 2
INNER = 2


def shifted(value, axis, steps):
    count = lax.axis_size(axis)
    leading, last = (max(0, -steps), min(count, count - steps))
    return lax.ppermute(value, axis, [(source, source + steps) for source in range(leading, last)])


def all_sum(value, axis):
    count = lax.axis_size(axis)
    copies = jnp.broadcast_to(value[None], (count,) + value.shape)
    return jnp.sum(lax.all_to_all(copies, axis, 0, 0, tiled=True), 0)


def lane_totals(copies, axis, lanes):
    count = lax.axis_size(axis)
    received = lax.all_to_all(copies, axis, 0, 0, tiled=True)
    return jnp.dot(received.T, jnp.ones((count, lanes), jnp.float32), precision=lax.Precision.HIGHEST)


def on_device(band_blocks, distant_block_slots, far_rows, far_columns, far_counts):
    rows_dev = band_blocks.shape[0]
    block_size = band_blocks.shape[2]
    band_count = lax.axis_size("band")
    row_count = lax.axis_size("row")
    offset = lax.axis_index("band")
    row_index = lax.axis_index("row")
    blocks = band_blocks[:, 0]
    distant_local_part = distant_block_slots[0, 0]
    local_row_values = far_rows[0, 0]
    columns_local = far_columns[0, 0]
    counts = far_counts[0, 0]
    slots = local_row_values.shape[1]
    live_mask = (jnp.arange(slots)[None, :] < counts[:, None]).astype(jnp.float32)[..., None]
    block_ids = row_index * rows_dev + jnp.arange(rows_dev)
    valid_mask = (block_ids + offset < row_count * rows_dev).astype(jnp.float32)[:, None]
    upper_mask = (offset > 0).astype(jnp.float32)
    targets = jnp.arange(rows_dev)[None, :]
    pick_in = (local_row_values.reshape(-1)[:, None] == targets).astype(jnp.float32)
    pick_rows = pick_in.astype(jnp.bfloat16)

    def picked(selection, vector):
        product = jnp.dot(selection, vector, preferred_element_type=jnp.float32)
        return product.reshape(row_count, slots, block_size)

    def multiply(vector, wanted=None):
        narrow_band_part = vector.astype(jnp.bfloat16)
        ahead_rows = shifted(narrow_band_part[:band_count], "row", -1)
        extended = jnp.concatenate([narrow_band_part, ahead_rows], 0)
        columns = lax.dynamic_slice_in_dim(extended, offset, rows_dev, 0)
        forward = (
            jnp.einsum("kij,kj->ki", blocks, columns, preferred_element_type=jnp.float32)
            * valid_mask
        )
        backward = jnp.einsum(
            "kij,ki->kj", blocks, narrow_band_part, preferred_element_type=jnp.float32
        ) * (valid_mask * upper_mask)
        spread = lax.dynamic_update_slice_in_dim(
            jnp.zeros((rows_dev + band_count, block_size), jnp.float32), backward, offset, 0
        )
        far_backward = (
            jnp.einsum(
                "nquo,nqu->nqo",
                distant_local_part,
                picked(pick_rows, narrow_band_part).astype(jnp.bfloat16),
                preferred_element_type=jnp.float32,
            )
            * live_mask
        )
        if wanted is None:
            column_row = jnp.zeros((row_count, 1, block_size), jnp.float32)
            column_row = column_row.at[:, 0, :slots].set(columns_local.astype(jnp.float32))
            exchanged = lax.all_to_all(
                jnp.concatenate([column_row, far_backward], 1), "row", split_axis=0, concat_axis=0, tiled=True
            )
            wanted = jnp.round(exchanged[:, 0, :slots]).astype(jnp.int32)
            gathered_values = jnp.ones((row_count, slots, block_size), jnp.bfloat16)
            returned = exchanged[:, 1:]
        else:
            pick_out = (wanted.reshape(-1)[:, None] == targets).astype(jnp.bfloat16)
            outgoing = picked(pick_out, narrow_band_part)
            exchanged = lax.all_to_all(
                jnp.concatenate([outgoing, far_backward], 1), "row", split_axis=0, concat_axis=0, tiled=True
            )
            gathered_values = exchanged[:, :slots].astype(jnp.bfloat16)
            returned = exchanged[:, slots:]
        selection_output = (wanted.reshape(-1)[:, None] == targets).astype(jnp.float32)
        far_forward = (
            jnp.einsum(
                "oqht,oqt->oqh",
                distant_local_part,
                gathered_values,
                preferred_element_type=jnp.float32,
            )
            * live_mask
        )
        selection = jnp.concatenate([pick_in, selection_output], 0)
        far_parts = jnp.concatenate(
            [far_forward.reshape(-1, block_size), returned.reshape(-1, block_size)], 0
        )
        summed = forward + spread[:rows_dev]
        summed = summed + jnp.dot(selection.T, far_parts, precision=lax.Precision.HIGHEST)
        carried = shifted(spread[rows_dev:], "row", 1)
        summed = jnp.concatenate([summed[:band_count] + carried, summed[band_count:]], 0)
        return all_sum(summed, "band"), wanted

    row_sums, wanted = multiply(jnp.ones((rows_dev, block_size), jnp.float32))
    scaling = 1.0 / jnp.sqrt(row_sums)
    residual = jnp.zeros_like(scaling)
    for outer_step in range(OUTER):
        balance = scaling * multiply(scaling, wanted)[0]
        residual = 1.0 - balance
        scaled = residual / balance
        direction = scaled
        local_product = residual * scaled
        growth = jnp.ones_like(scaling)
        for inner_step in range(INNER):
            curved = scaling * multiply(scaling * direction, wanted)[0] + balance * direction
            last = inner_step + 1 == INNER
            parts = [direction * curved]
            if inner_step == 0:
                parts.append(local_product)
            if not last:
                parts.append(residual * curved / balance)
                parts.append(curved * curved / balance)
            stacked = jnp.stack(parts).reshape(len(parts), -1)
            copies = jnp.dot(
                jnp.ones((row_count, stacked.shape[1]), jnp.float32), stacked.T, precision=lax.Precision.HIGHEST
            )
            totals = lane_totals(copies, "row", block_size)
            curvature = totals[0]
            if inner_step == 0:
                current_residual_product = totals[1]
            step_size = current_residual_product / curvature
            growth = growth + step_size * direction
            residual = residual - step_size * curved
            if not last:
                cross, square = totals[-2], totals[-1]
                rho_next = current_residual_product - 2.0 * step_size * cross + step_size * step_size * square
                scaled = residual / balance
                direction = scaled + rho_next / current_residual_product * direction
                current_residual_product = rho_next
        scaling = scaling * growth
    return (scaling, residual)


def solution(mesh):
    return jax.shard_map(
        on_device,
        mesh=mesh,
        in_specs=(
            P("row", "band", None, None),
            P("row", "band", None, None, None, None),
            P("row", "band", None, None),
            P("row", "band", None, None),
            P("row", "band", None),
        ),
        out_specs=(P("row", None), P("row", None)),
        check_vma=False,
    )
```

```python
import jax
import jax.numpy as jnp
from jax import lax
from jax.sharding import PartitionSpec as P

OUTER = 2
INNER = 2


def shifted(value, axis, steps):
    count = lax.axis_size(axis)
    leading, last = (max(0, -steps), min(count, count - steps))
    return lax.ppermute(value, axis, [(source, source + steps) for source in range(leading, last)])


def all_sum(value, axis):
    count = lax.axis_size(axis)
    copies = jnp.broadcast_to(value[None], (count,) + value.shape)
    return jnp.sum(lax.all_to_all(copies, axis, 0, 0, tiled=True), 0)


def lane_totals(copies, axis, lanes):
    count = lax.axis_size(axis)
    received = lax.all_to_all(copies, axis, 0, 0, tiled=True)
    return jnp.dot(received.T, jnp.ones((count, lanes), jnp.float32), precision=lax.Precision.HIGHEST)


def on_device(band_blocks, distant_block_slots, far_rows, far_columns, far_counts):
    rows_dev = band_blocks.shape[0]
    block_size = band_blocks.shape[2]
    band_count = lax.axis_size("band")
    row_count = lax.axis_size("row")
    offset = lax.axis_index("band")
    row_index = lax.axis_index("row")
    blocks = band_blocks[:, 0]
    distant_local_part = distant_block_slots[0, 0]
    local_row_values = far_rows[0, 0]
    columns_local = far_columns[0, 0]
    counts = far_counts[0, 0]
    slots = local_row_values.shape[1]
    live_mask = (jnp.arange(slots)[None, :] < counts[:, None]).astype(jnp.float32)[..., None]
    block_ids = row_index * rows_dev + jnp.arange(rows_dev)
    valid_mask = (block_ids + offset < row_count * rows_dev).astype(jnp.float32)[:, None]
    upper_mask = (offset > 0).astype(jnp.float32)
    targets = jnp.arange(rows_dev)[None, :]
    pick_in = (local_row_values.reshape(-1)[:, None] == targets).astype(jnp.float32)
    pick_rows = pick_in.astype(jnp.bfloat16)
    identity_blocks = jnp.broadcast_to(
        jnp.eye(block_size, dtype=jnp.bfloat16), (row_count, slots, block_size, block_size)
    )
    exchange_blocks = jnp.concatenate([identity_blocks, distant_local_part], 1)
    exchange_mask = jnp.concatenate([jnp.ones_like(live_mask), live_mask], 1)

    def picked(selection, vector):
        product = jnp.dot(selection, vector, preferred_element_type=jnp.float32)
        return product.reshape(row_count, slots, block_size)

    def multiply(vector, wanted=None):
        narrow_band_part = vector.astype(jnp.bfloat16)
        ahead_rows = shifted(narrow_band_part[:band_count], "row", -1)
        extended = jnp.concatenate([narrow_band_part, ahead_rows], 0)
        columns = lax.dynamic_slice_in_dim(extended, offset, rows_dev, 0)
        forward = (
            jnp.einsum("kij,kj->ki", blocks, columns, preferred_element_type=jnp.float32)
            * valid_mask
        )
        backward = jnp.einsum(
            "kij,ki->kj", blocks, narrow_band_part, preferred_element_type=jnp.float32
        ) * (valid_mask * upper_mask)
        spread = lax.dynamic_update_slice_in_dim(
            jnp.zeros((rows_dev + band_count, block_size), jnp.float32), backward, offset, 0
        )
        far_backward = (
            jnp.einsum(
                "nquo,nqu->nqo",
                distant_local_part,
                picked(pick_rows, narrow_band_part).astype(jnp.bfloat16),
                preferred_element_type=jnp.float32,
            )
            * live_mask
        )
        if wanted is None:
            column_row = jnp.zeros((row_count, 1, block_size), jnp.float32)
            column_row = column_row.at[:, 0, :slots].set(columns_local.astype(jnp.float32))
            exchanged = lax.all_to_all(
                jnp.concatenate([column_row, far_backward], 1), "row", split_axis=0, concat_axis=0, tiled=True
            )
            wanted = jnp.round(exchanged[:, 0, :slots]).astype(jnp.int32)
            gathered_values = jnp.ones((row_count, slots, block_size), jnp.bfloat16)
            returned = exchanged[:, 1:]
        else:
            selection_both = jnp.concatenate(
                [wanted[..., None] == targets[None], local_row_values[..., None] == targets[None]], 1
            ).astype(jnp.bfloat16)
            vectors = jnp.dot(
                selection_both.reshape(-1, rows_dev), narrow_band_part, preferred_element_type=jnp.float32
            ).reshape(row_count, 2 * slots, block_size)
            payload = (
                jnp.einsum(
                    "nquo,nqu->nqo",
                    exchange_blocks,
                    vectors.astype(jnp.bfloat16),
                    preferred_element_type=jnp.float32,
                )
                * exchange_mask
            )
            exchanged = lax.all_to_all(payload, "row", split_axis=0, concat_axis=0, tiled=True)
            gathered_values = exchanged[:, :slots].astype(jnp.bfloat16)
            returned = exchanged[:, slots:]
        selection_output = (wanted.reshape(-1)[:, None] == targets).astype(jnp.float32)
        far_forward = (
            jnp.einsum(
                "oqht,oqt->oqh",
                distant_local_part,
                gathered_values,
                preferred_element_type=jnp.float32,
            )
            * live_mask
        )
        selection = jnp.concatenate([pick_in, selection_output], 0)
        far_parts = jnp.concatenate(
            [far_forward.reshape(-1, block_size), returned.reshape(-1, block_size)], 0
        )
        summed = forward + spread[:rows_dev]
        summed = summed + jnp.dot(selection.T, far_parts, precision=lax.Precision.HIGHEST)
        carried = shifted(spread[rows_dev:], "row", 1)
        summed = jnp.concatenate([summed[:band_count] + carried, summed[band_count:]], 0)
        return all_sum(summed, "band"), wanted

    row_sums, wanted = multiply(jnp.ones((rows_dev, block_size), jnp.float32))
    scaling = 1.0 / jnp.sqrt(row_sums)
    residual = jnp.zeros_like(scaling)
    for outer_step in range(OUTER):
        balance = scaling * multiply(scaling, wanted)[0]
        residual = 1.0 - balance
        scaled = residual / balance
        direction = scaled
        local_product = residual * scaled
        growth = jnp.ones_like(scaling)
        for inner_step in range(INNER):
            curved = scaling * multiply(scaling * direction, wanted)[0] + balance * direction
            last = inner_step + 1 == INNER
            parts = [direction * curved]
            if inner_step == 0:
                parts.append(local_product)
            if not last:
                parts.append(residual * curved / balance)
                parts.append(curved * curved / balance)
            stacked = jnp.stack(parts).reshape(len(parts), -1)
            copies = jnp.dot(
                jnp.ones((row_count, stacked.shape[1]), jnp.float32), stacked.T, precision=lax.Precision.HIGHEST
            )
            totals = lane_totals(copies, "row", block_size)
            curvature = totals[0]
            if inner_step == 0:
                current_residual_product = totals[1]
            step_size = current_residual_product / curvature
            growth = growth + step_size * direction
            residual = residual - step_size * curved
            if not last:
                cross, square = totals[-2], totals[-1]
                rho_next = current_residual_product - 2.0 * step_size * cross + step_size * step_size * square
                scaled = residual / balance
                direction = scaled + rho_next / current_residual_product * direction
                current_residual_product = rho_next
        scaling = scaling * growth
    return (scaling, residual)


def solution(mesh):
    return jax.shard_map(
        on_device,
        mesh=mesh,
        in_specs=(
            P("row", "band", None, None),
            P("row", "band", None, None, None, None),
            P("row", "band", None, None),
            P("row", "band", None, None),
            P("row", "band", None),
        ),
        out_specs=(P("row", None), P("row", None)),
        check_vma=False,
    )
```

```python
import jax
import jax.numpy as jnp
from jax import lax
from jax.sharding import PartitionSpec as P

OUTER = 2
INNER = 2


def shifted(value, axis, steps):
    count = lax.axis_size(axis)
    leading, last = (max(0, -steps), min(count, count - steps))
    return lax.ppermute(value, axis, [(source, source + steps) for source in range(leading, last)])


def all_sum(value, axis):
    count = lax.axis_size(axis)
    copies = jnp.broadcast_to(value[None], (count,) + value.shape)
    return jnp.sum(lax.all_to_all(copies, axis, 0, 0, tiled=True), 0)


def lane_totals(copies, axis, lanes):
    count = lax.axis_size(axis)
    received = lax.all_to_all(copies, axis, 0, 0, tiled=True)
    return jnp.dot(received.T, jnp.ones((count, lanes), jnp.float32), precision=lax.Precision.HIGH)


def on_device(band_blocks, distant_block_slots, far_rows, far_columns, far_counts):
    rows_dev = band_blocks.shape[0]
    block_size = band_blocks.shape[2]
    band_count = lax.axis_size("band")
    row_count = lax.axis_size("row")
    offset = lax.axis_index("band")
    row_index = lax.axis_index("row")
    blocks = band_blocks[:, 0]
    distant_local_part = distant_block_slots[0, 0]
    local_row_values = far_rows[0, 0]
    columns_local = far_columns[0, 0]
    counts = far_counts[0, 0]
    slots = local_row_values.shape[1]
    live_mask = (jnp.arange(slots)[None, :] < counts[:, None]).astype(jnp.float32)[..., None]
    block_ids = row_index * rows_dev + jnp.arange(rows_dev)
    valid_mask = (block_ids + offset < row_count * rows_dev).astype(jnp.float32)[:, None]
    upper_mask = (offset > 0).astype(jnp.float32)
    targets = jnp.arange(rows_dev)[None, :]
    pick_in = (local_row_values.reshape(-1)[:, None] == targets).astype(jnp.float32)
    pick_rows = pick_in.astype(jnp.bfloat16)

    def picked(selection, vector):
        product = jnp.dot(selection, vector, preferred_element_type=jnp.float32)
        return product.reshape(row_count, slots, block_size)

    def multiply(vector, wanted=None):
        narrow_band_part = vector.astype(jnp.bfloat16)
        ahead_rows = shifted(narrow_band_part[:band_count], "row", -1)
        extended = jnp.concatenate([narrow_band_part, ahead_rows], 0)
        columns = lax.dynamic_slice_in_dim(extended, offset, rows_dev, 0)
        forward = (
            jnp.einsum("kij,kj->ki", blocks, columns, preferred_element_type=jnp.float32)
            * valid_mask
        )
        backward = jnp.einsum(
            "kij,ki->kj", blocks, narrow_band_part, preferred_element_type=jnp.float32
        ) * (valid_mask * upper_mask)
        spread = lax.dynamic_update_slice_in_dim(
            jnp.zeros((rows_dev + band_count, block_size), jnp.float32), backward, offset, 0
        )
        far_backward = (
            jnp.einsum(
                "nquo,nqu->nqo",
                distant_local_part,
                picked(pick_rows, narrow_band_part).astype(jnp.bfloat16),
                preferred_element_type=jnp.float32,
            )
            * live_mask
        )
        if wanted is None:
            column_row = jnp.zeros((row_count, 1, block_size), jnp.float32)
            column_row = column_row.at[:, 0, :slots].set(columns_local.astype(jnp.float32))
            exchanged = lax.all_to_all(
                jnp.concatenate([column_row, far_backward], 1), "row", split_axis=0, concat_axis=0, tiled=True
            )
            wanted = jnp.round(exchanged[:, 0, :slots]).astype(jnp.int32)
            gathered_values = jnp.ones((row_count, slots, block_size), jnp.bfloat16)
            returned = exchanged[:, 1:]
        else:
            pick_out = (wanted.reshape(-1)[:, None] == targets).astype(jnp.bfloat16)
            outgoing = picked(pick_out, narrow_band_part)
            exchanged = lax.all_to_all(
                jnp.concatenate([outgoing, far_backward], 1), "row", split_axis=0, concat_axis=0, tiled=True
            )
            gathered_values = exchanged[:, :slots].astype(jnp.bfloat16)
            returned = exchanged[:, slots:]
        selection_output = (wanted.reshape(-1)[:, None] == targets).astype(jnp.float32)
        far_forward = (
            jnp.einsum(
                "oqht,oqt->oqh",
                distant_local_part,
                gathered_values,
                preferred_element_type=jnp.float32,
            )
            * live_mask
        )
        selection = jnp.concatenate([pick_in, selection_output], 0)
        far_parts = jnp.concatenate(
            [far_forward.reshape(-1, block_size), returned.reshape(-1, block_size)], 0
        )
        summed = forward + spread[:rows_dev]
        summed = summed + jnp.dot(selection.T, far_parts, precision=lax.Precision.HIGH)
        carried = shifted(spread[rows_dev:], "row", 1)
        summed = jnp.concatenate([summed[:band_count] + carried, summed[band_count:]], 0)
        return all_sum(summed, "band"), wanted

    row_sums, wanted = multiply(jnp.ones((rows_dev, block_size), jnp.float32))
    scaling = 1.0 / jnp.sqrt(row_sums)
    residual = jnp.zeros_like(scaling)
    for outer_step in range(OUTER):
        balance = scaling * multiply(scaling, wanted)[0]
        residual = 1.0 - balance
        scaled = residual / balance
        direction = scaled
        local_product = residual * scaled
        growth = jnp.ones_like(scaling)
        for inner_step in range(INNER):
            curved = scaling * multiply(scaling * direction, wanted)[0] + balance * direction
            last = inner_step + 1 == INNER
            parts = [direction * curved]
            if inner_step == 0:
                parts.append(local_product)
            if not last:
                parts.append(residual * curved / balance)
                parts.append(curved * curved / balance)
            stacked = jnp.stack(parts).reshape(len(parts), -1)
            copies = jnp.dot(
                jnp.ones((row_count, stacked.shape[1]), jnp.float32), stacked.T, precision=lax.Precision.HIGH
            )
            totals = lane_totals(copies, "row", block_size)
            curvature = totals[0]
            if inner_step == 0:
                current_residual_product = totals[1]
            step_size = current_residual_product / curvature
            growth = growth + step_size * direction
            residual = residual - step_size * curved
            if not last:
                cross, square = totals[-2], totals[-1]
                rho_next = current_residual_product - 2.0 * step_size * cross + step_size * step_size * square
                scaled = residual / balance
                direction = scaled + rho_next / current_residual_product * direction
                current_residual_product = rho_next
        scaling = scaling * growth
    return (scaling, residual)


def solution(mesh):
    return jax.shard_map(
        on_device,
        mesh=mesh,
        in_specs=(
            P("row", "band", None, None),
            P("row", "band", None, None, None, None),
            P("row", "band", None, None),
            P("row", "band", None, None),
            P("row", "band", None),
        ),
        out_specs=(P("row", None), P("row", None)),
        check_vma=False,
    )
```
